512 devices in a mesh: row: 16 (over y, x_lo), col: 16 (over z, core), ka: 2 (over x_hi).
Axes of the slice: x: 4 (x_hi: 2, x_lo: 2; x = x_hi * 2 + x_lo), y: 8, z: 8, core: 2. Of those that a mesh axis runs over, the one named last changes fastest.
Arguments:
- pair: bfloat16 [512, 512, 128], P('row', ('col', 'ka')), may hold values from -6 to 6
- pair_mask: int32 [512, 512], P('row', ('col', 'ka')), may hold values from 0 to 1, as said below
- w_in: bfloat16 [2, 128, 512], replicated, may hold values from -0.5 to 0.5
- w_gate: bfloat16 [2, 128, 128], replicated, may hold values from -0.5 to 0.5
- w_out: bfloat16 [2, 128, 128], replicated, may hold values from -0.5 to 0.5
Outputs:
- updated: bfloat16 [512, 512, 128], P('row', ('col', 'ka'))
The draws below stay inside these ranges and needn't reach their ends.
Inputs may be any that keep to these rules, and one draw needn't show every extreme that they name: pair_mask[i, j] = v[i] v[j] for a per-token 0/1 validity v; within each aligned run of 16 tokens the real tokens come first and there is at least one.
All inputs are finite; a program needn't handle non-finite values.
Results may differ from the reference program's by a relative error of at most 0.014.
Values may be sent and summed in bfloat16 or wider, within the bound.
No kernel may reach another device: no remote copies, remote signals or barrier semaphores. Data moves between devices by JAX's collectives and lax.ppermute only.
A program may use at most 64 MiB of HBM per device.

```python
import jax
import jax.numpy as jnp
from jax import lax

C = 128
CH = 128
CHAIN = 16
TOKENS = 512


def draw_pair_mask(key, part):
    runs = TOKENS // CHAIN
    counts = jax.random.randint(key, (runs,), 1, CHAIN + 1)
    counts = jnp.where(jnp.arange(runs) == 0, CHAIN // 2, counts)
    position = jnp.arange(TOKENS)
    validity = (position % CHAIN < counts[position // CHAIN]).astype(jnp.int32)
    return (validity[:, None] * validity[None, :]).astype(jnp.int32)


def levels(stream_key, dims, shards, low, largest):
    level = 1.0
    for axis_at, shards_of in shards:
        draws = jax.random.uniform(jax.random.fold_in(jax.random.fold_in(stream_key, 6), axis_at), (shards_of,), jnp.float32, low / len(shards), largest / len(shards))
        level = level * jnp.repeat(jnp.exp(draws), dims[axis_at] // shards_of).reshape((-1,) + (1,) * (len(dims) - 1 - axis_at))
    return level


def normal_values(stream_key, dims, spread, limit, pieces=(), held_as=jnp.bfloat16):
    array = jax.random.normal(stream_key, dims, jnp.float32) * spread
    if len(pieces) > 0:
        array = levels(stream_key, dims, pieces, -0.22, 0.18) * array
    return jnp.clip(array, min=-limit, max=limit).astype(held_as)


def setup_inputs(seed: int = 0) -> dict:
    streams_of = jax.random.split(jax.random.key(seed), 6)
    return {
        "pair": normal_values(streams_of[0], (TOKENS, TOKENS, C), 1.0, 6.0, ((0, 16), (1, 32))),
        "pair_mask": draw_pair_mask(jax.random.fold_in(streams_of[5], 71), 0),
        "w_in": normal_values(streams_of[2], (2, C, 4 * CH), C ** -0.5, 0.5),
        "w_gate": normal_values(streams_of[3], (2, C, C), C ** -0.5, 0.5),
        "w_out": normal_values(streams_of[4], (2, CH, C), CH ** -0.5, 0.5),
    }


def layer_norm(value):
    mean = lax.optimization_barrier(jnp.mean(value, axis=-1, keepdims=True))
    centred = value - mean
    var = lax.optimization_barrier(jnp.mean(centred * centred, axis=-1, keepdims=True))
    return centred / jnp.sqrt(var + 1e-05)

def prepare(pair, valid, weight_in, weight_gate):
    normed = layer_norm(pair.astype(jnp.float32)).astype(jnp.bfloat16)
    flat = normed.reshape(-1, normed.shape[-1])
    proj = jnp.dot(flat, weight_in, preferred_element_type=jnp.float32)
    proj = proj.reshape(pair.shape[0], pair.shape[1], -1)
    width = proj.shape[-1] // 4
    left = (jax.nn.sigmoid(proj[..., :width]) * proj[..., width:2 * width] * valid).astype(jnp.bfloat16)
    right = (jax.nn.sigmoid(proj[..., 2 * width:3 * width]) * proj[..., 3 * width:] * valid).astype(jnp.bfloat16)
    gate = jax.nn.sigmoid(jnp.dot(flat, weight_gate, preferred_element_type=jnp.float32))
    gate = gate.reshape(pair.shape[0], pair.shape[1], -1)
    return (left, right, gate)

def finish(pair, tri, gate, weight_out):
    normed = layer_norm(tri).astype(jnp.bfloat16)
    flat = normed.reshape(-1, normed.shape[-1])
    proj = jnp.dot(flat, weight_out, preferred_element_type=jnp.float32)
    proj = proj.reshape(pair.shape[0], pair.shape[1], -1)
    return (pair.astype(jnp.float32) + gate * proj).astype(jnp.bfloat16)

def reference(pair, pair_mask, w_in, w_gate, w_out):
    valid = pair_mask.astype(jnp.float32)[..., None]
    left, right, gate = prepare(pair, valid, w_in[0], w_gate[0])
    tri = jnp.einsum('ikc,jkc->ijc', left.astype(jnp.float32), right.astype(jnp.float32))
    middle = finish(pair, tri, gate, w_out[0])
    left, right, gate = prepare(middle, valid, w_in[1], w_gate[1])
    tri = jnp.einsum('kic,kjc->ijc', left.astype(jnp.float32), right.astype(jnp.float32))
    return finish(middle, tri, gate, w_out[1])
```

```python
import jax
import jax.numpy as jnp
from jax import lax
from jax.sharding import PartitionSpec as P


def layer_norm(value):
    mean = jnp.mean(value, axis=-1, keepdims=True)
    centred = value - mean
    var = jnp.mean(centred * centred, axis=-1, keepdims=True)
    return centred / jnp.sqrt(var + 1e-05)


def prepare(pair, valid, weight_in, weight_gate):
    normed = layer_norm(pair.astype(jnp.float32)).astype(jnp.bfloat16)
    proj = jnp.einsum("ijc,cd->ijd", normed, weight_in, preferred_element_type=jnp.float32)
    width = proj.shape[-1] // 4
    left = (jax.nn.sigmoid(proj[..., :width]) * proj[..., width : 2 * width] * valid).astype(
        jnp.bfloat16
    )
    right = (
        jax.nn.sigmoid(proj[..., 2 * width : 3 * width]) * proj[..., 3 * width :] * valid
    ).astype(jnp.bfloat16)
    gate = jax.nn.sigmoid(
        jnp.einsum("ijc,cd->ijd", normed, weight_gate, preferred_element_type=jnp.float32)
    )
    return (left, right, gate)


def finish(pair, tri, gate, weight_out):
    normed = layer_norm(tri).astype(jnp.bfloat16)
    proj = jnp.einsum("ijc,cd->ijd", normed, weight_out, preferred_element_type=jnp.float32)
    return (pair.astype(jnp.float32) + gate * proj).astype(jnp.bfloat16)


def transpose_tiles(value, n):
    perm = [(r * n + c, c * n + r) for r in range(n) for c in range(n)]
    return lax.ppermute(value, ("row", "col"), perm)


def on_device(n, pair, pair_mask, w_in, w_gate, w_out):
    valid = pair_mask.astype(jnp.float32)[..., None]
    left, right, gate = prepare(pair, valid, w_in[0], w_gate[0])
    left_rows = lax.all_gather(left, "col", axis=1, tiled=True)
    right_diag = lax.all_gather(transpose_tiles(right, n), "row", axis=1, tiled=True)
    partial_value = jnp.einsum(
        "ikc,jkc->ijc", left_rows, right_diag, preferred_element_type=jnp.float32
    )
    tri = lax.psum_scatter(
        partial_value.astype(jnp.bfloat16), "ka", scatter_dimension=1, tiled=True
    ).astype(jnp.float32)
    middle = finish(pair, tri, gate, w_out[0])
    left, right, gate = prepare(middle, valid, w_in[1], w_gate[1])
    right_cols = lax.all_gather(right, "row", axis=0, tiled=True)
    left_half = lax.all_gather(transpose_tiles(left, n), "col", axis=0, tiled=True)
    left_diag = lax.all_gather(left_half, "ka", axis=1, tiled=True)
    tri = jnp.einsum("kic,kjc->ijc", left_diag, right_cols, preferred_element_type=jnp.float32)
    return finish(middle, tri, gate, w_out[1])


def solution(mesh):
    n = mesh.shape["row"]
    assert mesh.shape["col"] == n
    placed = (P("row", ("col", "ka"), None), P("row", ("col", "ka")), P(), P(), P())
    return jax.shard_map(
        lambda *a: on_device(n, *a),
        mesh=mesh,
        in_specs=placed,
        out_specs=P("row", ("col", "ka"), None),
        check_vma=False,
    )
```

```python
import jax
import jax.numpy as jnp
from jax import lax
from jax.sharding import PartitionSpec as P


def layer_norm(value):
    mean = jnp.mean(value, axis=-1, keepdims=True)
    centred = value - mean
    var = jnp.mean(centred * centred, axis=-1, keepdims=True)
    return centred / jnp.sqrt(var + 1e-05)


def prepare(pair, valid, weight_in, weight_gate):
    normed = layer_norm(pair.astype(jnp.float32)).astype(jnp.bfloat16)
    proj = jnp.einsum("ijc,cd->ijd", normed, weight_in, preferred_element_type=jnp.float32)
    width = proj.shape[-1] // 4
    left = (jax.nn.sigmoid(proj[..., :width]) * proj[..., width : 2 * width] * valid).astype(
        jnp.bfloat16
    )
    right = (
        jax.nn.sigmoid(proj[..., 2 * width : 3 * width]) * proj[..., 3 * width :] * valid
    ).astype(jnp.bfloat16)
    gate = jax.nn.sigmoid(
        jnp.einsum("ijc,cd->ijd", normed, weight_gate, preferred_element_type=jnp.float32)
    )
    return (left, right, gate)


def finish(pair, tri, gate, weight_out):
    normed = layer_norm(tri).astype(jnp.bfloat16)
    proj = jnp.einsum("ijc,cd->ijd", normed, weight_out, preferred_element_type=jnp.float32)
    return (pair.astype(jnp.float32) + gate * proj).astype(jnp.bfloat16)


def transpose_tiles(value, n):
    perm = [(r * n + c, c * n + r) for r in range(n) for c in range(n)]
    return lax.ppermute(value, ("row", "col"), perm)


def gather_a2a(value, axis_name, n, axis):
    copies = jnp.broadcast_to(value[None], (n,) + value.shape)
    got = lax.all_to_all(copies, axis_name, 0, 0, tiled=False)
    got = jnp.moveaxis(got, 0, axis)
    return got.reshape(value.shape[:axis] + (n * value.shape[axis],) + value.shape[axis + 1 :])


def on_device(n, pair, pair_mask, w_in, w_gate, w_out):
    valid = pair_mask.astype(jnp.float32)[..., None]
    left, right, gate = prepare(pair, valid, w_in[0], w_gate[0])
    left_rows = lax.all_gather(left, "col", axis=1, tiled=True)
    right_diag = gather_a2a(transpose_tiles(right, n), "row", n, 1)
    partial_value = jnp.einsum(
        "ikc,jkc->ijc", left_rows, right_diag, preferred_element_type=jnp.float32
    )
    tri = lax.psum_scatter(
        partial_value.astype(jnp.bfloat16), "ka", scatter_dimension=1, tiled=True
    ).astype(jnp.float32)
    middle = finish(pair, tri, gate, w_out[0])
    left, right, gate = prepare(middle, valid, w_in[1], w_gate[1])
    right_cols = gather_a2a(right, "row", n, 0)
    left_half = lax.all_gather(transpose_tiles(left, n), "col", axis=0, tiled=True)
    left_diag = lax.all_gather(left_half, "ka", axis=1, tiled=True)
    tri = jnp.einsum("kic,kjc->ijc", left_diag, right_cols, preferred_element_type=jnp.float32)
    return finish(middle, tri, gate, w_out[1])


def solution(mesh):
    n = mesh.shape["row"]
    assert mesh.shape["col"] == n
    placed = (P("row", ("col", "ka"), None), P("row", ("col", "ka")), P(), P(), P())
    return jax.shard_map(
        lambda *a: on_device(n, *a),
        mesh=mesh,
        in_specs=placed,
        out_specs=P("row", ("col", "ka"), None),
        check_vma=False,
    )
```

```python
import jax
import jax.numpy as jnp
from jax import lax
from jax.sharding import PartitionSpec as P


def layer_norm(value):
    mean = jnp.mean(value, axis=-1, keepdims=True)
    centred = value - mean
    var = jnp.mean(centred * centred, axis=-1, keepdims=True)
    return centred / jnp.sqrt(var + 1e-05)


def prepare(pair, valid, weight_in, weight_gate):
    normed = layer_norm(pair.astype(jnp.float32)).astype(jnp.bfloat16)
    proj = jnp.einsum("ijc,cd->ijd", normed, weight_in, preferred_element_type=jnp.float32)
    width = proj.shape[-1] // 4
    left = (jax.nn.sigmoid(proj[..., :width]) * proj[..., width : 2 * width] * valid).astype(
        jnp.bfloat16
    )
    right = (
        jax.nn.sigmoid(proj[..., 2 * width : 3 * width]) * proj[..., 3 * width :] * valid
    ).astype(jnp.bfloat16)
    gate = jax.nn.sigmoid(
        jnp.einsum("ijc,cd->ijd", normed, weight_gate, preferred_element_type=jnp.float32)
    )
    return (left, right, gate)


def finish(pair, tri, gate, weight_out):
    normed = layer_norm(tri).astype(jnp.bfloat16)
    proj = jnp.einsum("ijc,cd->ijd", normed, weight_out, preferred_element_type=jnp.float32)
    return (pair.astype(jnp.float32) + gate * proj).astype(jnp.bfloat16)


def transpose_tiles(value, n):
    perm = [(r * n + c, c * n + r) for r in range(n) for c in range(n)]
    return lax.ppermute(value, ("row", "col"), perm)


def gather_a2a(value, axis_name, n, axis):
    copies = jnp.broadcast_to(value[None], (n,) + value.shape)
    got = lax.all_to_all(copies, axis_name, 0, 0, tiled=False)
    got = jnp.moveaxis(got, 0, axis)
    return got.reshape(value.shape[:axis] + (n * value.shape[axis],) + value.shape[axis + 1 :])


def sum_over_ka(partial_value):
    half = partial_value.shape[1] // 2
    me = lax.axis_index("ka")
    mine = lax.dynamic_slice_in_dim(partial_value, me * half, half, axis=1)
    theirs = lax.dynamic_slice_in_dim(partial_value, (1 - me) * half, half, axis=1)
    got = lax.ppermute(theirs.astype(jnp.bfloat16), "ka", [(0, 1), (1, 0)])
    return mine + got.astype(jnp.float32)


def on_device(n, pair, pair_mask, w_in, w_gate, w_out):
    valid = pair_mask.astype(jnp.float32)[..., None]
    left, right, gate = prepare(pair, valid, w_in[0], w_gate[0])
    left_rows = lax.all_gather(left, "col", axis=1, tiled=True)
    right_diag = gather_a2a(transpose_tiles(right, n), "row", n, 1)
    partial_value = jnp.einsum(
        "ikc,jkc->ijc", left_rows, right_diag, preferred_element_type=jnp.float32
    )
    tri = sum_over_ka(partial_value)
    middle = finish(pair, tri, gate, w_out[0])
    left, right, gate = prepare(middle, valid, w_in[1], w_gate[1])
    right_cols = gather_a2a(right, "row", n, 0)
    left_half = lax.all_gather(transpose_tiles(left, n), "col", axis=0, tiled=True)
    left_diag = lax.all_gather(left_half, "ka", axis=1, tiled=True)
    tri = jnp.einsum("kic,kjc->ijc", left_diag, right_cols, preferred_element_type=jnp.float32)
    return finish(middle, tri, gate, w_out[1])


def solution(mesh):
    n = mesh.shape["row"]
    assert mesh.shape["col"] == n
    placed = (P("row", ("col", "ka"), None), P("row", ("col", "ka")), P(), P(), P())
    return jax.shard_map(
        lambda *a: on_device(n, *a),
        mesh=mesh,
        in_specs=placed,
        out_specs=P("row", ("col", "ka"), None),
        check_vma=False,
    )
```

```python
import jax
import jax.numpy as jnp
from jax import lax
from jax.sharding import PartitionSpec as P


def layer_norm(value):
    mean = jnp.mean(value, axis=-1, keepdims=True)
    centred = value - mean
    var = jnp.mean(centred * centred, axis=-1, keepdims=True)
    return centred / jnp.sqrt(var + 1e-05)


def prepare(pair, valid, weight_in, weight_gate):
    normed = layer_norm(pair.astype(jnp.float32)).astype(jnp.bfloat16)
    proj = jnp.einsum("ijc,cd->ijd", normed, weight_in, preferred_element_type=jnp.float32)
    width = proj.shape[-1] // 4
    left = (jax.nn.sigmoid(proj[..., :width]) * proj[..., width : 2 * width] * valid).astype(
        jnp.bfloat16
    )
    right = (
        jax.nn.sigmoid(proj[..., 2 * width : 3 * width]) * proj[..., 3 * width :] * valid
    ).astype(jnp.bfloat16)
    gate = jax.nn.sigmoid(
        jnp.einsum("ijc,cd->ijd", normed, weight_gate, preferred_element_type=jnp.float32)
    )
    return (left, right, gate)


def finish(pair, tri, gate, weight_out):
    normed = layer_norm(tri).astype(jnp.bfloat16)
    proj = jnp.einsum("ijc,cd->ijd", normed, weight_out, preferred_element_type=jnp.float32)
    return (pair.astype(jnp.float32) + gate * proj).astype(jnp.bfloat16)


def transpose_tiles(value, n):
    perm = [(r * n + c, c * n + r) for r in range(n) for c in range(n)]
    return lax.ppermute(value, ("row", "col"), perm)


def gather_a2a(value, axis_name, n, axis):
    copies = jnp.broadcast_to(value[None], (n,) + value.shape)
    got = lax.all_to_all(copies, axis_name, 0, 0, tiled=False)
    got = jnp.moveaxis(got, 0, axis)
    return got.reshape(value.shape[:axis] + (n * value.shape[axis],) + value.shape[axis + 1 :])


def sum_over_ka(partial_value):
    half = partial_value.shape[1] // 2
    me = lax.axis_index("ka")
    mine = lax.dynamic_slice_in_dim(partial_value, me * half, half, axis=1)
    theirs = lax.dynamic_slice_in_dim(partial_value, (1 - me) * half, half, axis=1)
    got = lax.ppermute(theirs.astype(jnp.bfloat16), "ka", [(0, 1), (1, 0)])
    return mine + got.astype(jnp.float32)


def split_rows_over_ka(value):
    rows, cols = value.shape[0], value.shape[1]
    halves = value.reshape((2, rows // 2) + value.shape[1:])
    got = lax.all_to_all(halves, "ka", 0, 0, tiled=False)
    got = jnp.moveaxis(got, 0, 1)
    return got.reshape((rows // 2, 2 * cols) + value.shape[2:])


def on_device(n, pair, pair_mask, w_in, w_gate, w_out):
    valid = pair_mask.astype(jnp.float32)[..., None]
    left, right, gate = prepare(pair, valid, w_in[0], w_gate[0])
    left_rows = lax.all_gather(left, "col", axis=1, tiled=True)
    right_diag = gather_a2a(transpose_tiles(right, n), "row", n, 1)
    partial_value = jnp.einsum(
        "ikc,jkc->ijc", left_rows, right_diag, preferred_element_type=jnp.float32
    )
    tri = sum_over_ka(partial_value)
    middle = finish(pair, tri, gate, w_out[0])
    left, right, gate = prepare(middle, valid, w_in[1], w_gate[1])
    left_h, right_h = split_rows_over_ka(left), split_rows_over_ka(right)
    right_cols = gather_a2a(right_h, "row", n, 0)
    left_cols = lax.all_gather(transpose_tiles(left_h, n), "col", axis=0, tiled=True)
    partial_value = jnp.einsum(
        "kic,kjc->ijc", left_cols, right_cols, preferred_element_type=jnp.float32
    )
    tri = sum_over_ka(partial_value)
    return finish(middle, tri, gate, w_out[1])


def solution(mesh):
    n = mesh.shape["row"]
    assert mesh.shape["col"] == n
    placed = (P("row", ("col", "ka"), None), P("row", ("col", "ka")), P(), P(), P())
    return jax.shard_map(
        lambda *a: on_device(n, *a),
        mesh=mesh,
        in_specs=placed,
        out_specs=P("row", ("col", "ka"), None),
        check_vma=False,
    )
```

```python
import jax
import jax.numpy as jnp
from jax import lax
from jax.sharding import PartitionSpec as P


def layer_norm(value):
    mean = jnp.mean(value, axis=-1, keepdims=True)
    centred = value - mean
    var = jnp.mean(centred * centred, axis=-1, keepdims=True)
    return centred / jnp.sqrt(var + 1e-05)


def prepare(pair, valid, weight_in, weight_gate):
    normed = layer_norm(pair.astype(jnp.float32)).astype(jnp.bfloat16)
    proj = jnp.einsum("ijc,cd->ijd", normed, weight_in, preferred_element_type=jnp.float32)
    width = proj.shape[-1] // 4
    left = (jax.nn.sigmoid(proj[..., :width]) * proj[..., width : 2 * width] * valid).astype(
        jnp.bfloat16
    )
    right = (
        jax.nn.sigmoid(proj[..., 2 * width : 3 * width]) * proj[..., 3 * width :] * valid
    ).astype(jnp.bfloat16)
    gate = jax.nn.sigmoid(
        jnp.einsum("ijc,cd->ijd", normed, weight_gate, preferred_element_type=jnp.float32)
    )
    return (left, right, gate)


def finish(pair, tri, gate, weight_out):
    normed = layer_norm(tri).astype(jnp.bfloat16)
    proj = jnp.einsum("ijc,cd->ijd", normed, weight_out, preferred_element_type=jnp.float32)
    return (pair.astype(jnp.float32) + gate * proj).astype(jnp.bfloat16)


def transpose_tiles(value, n):
    perm = [(r * n + c, c * n + r) for r in range(n) for c in range(n)]
    return lax.ppermute(value, ("row", "col"), perm)


def gather_a2a(value, axis_name, n, axis):
    copies = jnp.broadcast_to(value[None], (n,) + value.shape)
    got = lax.all_to_all(copies, axis_name, 0, 0, tiled=False)
    got = jnp.moveaxis(got, 0, axis)
    return got.reshape(value.shape[:axis] + (n * value.shape[axis],) + value.shape[axis + 1 :])


def sum_over_ka(partial_value):
    half = partial_value.shape[1] // 2
    me = lax.axis_index("ka")
    mine = lax.dynamic_slice_in_dim(partial_value, me * half, half, axis=1)
    theirs = lax.dynamic_slice_in_dim(partial_value, (1 - me) * half, half, axis=1)
    got = lax.ppermute(theirs.astype(jnp.bfloat16), "ka", [(0, 1), (1, 0)])
    return mine + got.astype(jnp.float32)


def join_over_ka(value):
    me = lax.axis_index("ka")
    got = lax.ppermute(value, "ka", [(0, 1), (1, 0)])
    return jnp.where(
        me == 0, jnp.concatenate([value, got], axis=1), jnp.concatenate([got, value], axis=1)
    )


def on_device(n, pair, pair_mask, w_in, w_gate, w_out):
    valid = pair_mask.astype(jnp.float32)[..., None]
    left, right, gate = prepare(pair, valid, w_in[0], w_gate[0])
    left_rows = lax.all_gather(left, "col", axis=1, tiled=True)
    right_diag = gather_a2a(transpose_tiles(right, n), "row", n, 1)
    partial_value = jnp.einsum(
        "ikc,jkc->ijc", left_rows, right_diag, preferred_element_type=jnp.float32
    )
    tri = sum_over_ka(partial_value)
    middle = finish(pair, tri, gate, w_out[0])
    left, right, gate = prepare(middle, valid, w_in[1], w_gate[1])
    right_cols = gather_a2a(right, "row", n, 0)
    left_tile = join_over_ka(transpose_tiles(left, n))
    left_diag = lax.all_gather(left_tile, "col", axis=0, tiled=True)
    tri = jnp.einsum("kic,kjc->ijc", left_diag, right_cols, preferred_element_type=jnp.float32)
    return finish(middle, tri, gate, w_out[1])


def solution(mesh):
    n = mesh.shape["row"]
    assert mesh.shape["col"] == n
    placed = (P("row", ("col", "ka"), None), P("row", ("col", "ka")), P(), P(), P())
    return jax.shard_map(
        lambda *a: on_device(n, *a),
        mesh=mesh,
        in_specs=placed,
        out_specs=P("row", ("col", "ka"), None),
        check_vma=False,
    )
```

```python
import jax
import jax.numpy as jnp
from jax import lax
from jax.sharding import PartitionSpec as P


def layer_norm(value):
    mean = jnp.mean(value, axis=-1, keepdims=True)
    centred = value - mean
    var = jnp.mean(centred * centred, axis=-1, keepdims=True)
    return centred / jnp.sqrt(var + 1e-05)


def prepare(pair, valid, weight_in, weight_gate):
    normed = layer_norm(pair.astype(jnp.float32)).astype(jnp.bfloat16)
    proj = jnp.einsum("ijc,cd->ijd", normed, weight_in, preferred_element_type=jnp.float32)
    width = proj.shape[-1] // 4
    left = (jax.nn.sigmoid(proj[..., :width]) * proj[..., width : 2 * width] * valid).astype(
        jnp.bfloat16
    )
    right = (
        jax.nn.sigmoid(proj[..., 2 * width : 3 * width]) * proj[..., 3 * width :] * valid
    ).astype(jnp.bfloat16)
    gate = jax.nn.sigmoid(
        jnp.einsum("ijc,cd->ijd", normed, weight_gate, preferred_element_type=jnp.float32)
    )
    return (left, right, gate)


def finish(pair, tri, gate, weight_out):
    normed = layer_norm(tri).astype(jnp.bfloat16)
    proj = jnp.einsum("ijc,cd->ijd", normed, weight_out, preferred_element_type=jnp.float32)
    return (pair.astype(jnp.float32) + gate * proj).astype(jnp.bfloat16)


def transpose_tiles(value, n):
    perm = [(r * n + c, c * n + r) for r in range(n) for c in range(n)]
    return lax.ppermute(value, ("row", "col"), perm)


def gather_a2a(value, axis_name, n, axis):
    copies = jnp.broadcast_to(value[None], (n,) + value.shape)
    got = lax.all_to_all(copies, axis_name, 0, 0, tiled=False)
    got = jnp.moveaxis(got, 0, axis)
    return got.reshape(value.shape[:axis] + (n * value.shape[axis],) + value.shape[axis + 1 :])


def sum_over_ka(partial_value):
    half = partial_value.shape[1] // 2
    me = lax.axis_index("ka")
    mine = lax.dynamic_slice_in_dim(partial_value, me * half, half, axis=1)
    theirs = lax.dynamic_slice_in_dim(partial_value, (1 - me) * half, half, axis=1)
    got = lax.ppermute(theirs.astype(jnp.bfloat16), "ka", [(0, 1), (1, 0)])
    return mine + got.astype(jnp.float32)


def join_over_ka(value):
    me = lax.axis_index("ka")
    got = lax.ppermute(value, "ka", [(0, 1), (1, 0)])
    return jnp.where(
        me == 0, jnp.concatenate([value, got], axis=1), jnp.concatenate([got, value], axis=1)
    )


def on_device(n, pair, pair_mask, w_in, w_gate, w_out):
    valid = pair_mask.astype(jnp.float32)[..., None]
    left, right, gate = prepare(pair, valid, w_in[0], w_gate[0])
    left_rows = lax.all_gather(left, "col", axis=1, tiled=True)
    right_diag = gather_a2a(transpose_tiles(right, n), "row", n, 1)
    partial_value = jnp.einsum(
        "ikc,jkc->ijc", left_rows, right_diag, preferred_element_type=jnp.float32
    )
    tri = sum_over_ka(partial_value)
    middle = finish(pair, tri, gate, w_out[0])
    left, right, gate = prepare(middle, valid, w_in[1], w_gate[1])
    right_cols = gather_a2a(right, "row", n, 0)
    left_tile = join_over_ka(transpose_tiles(left, n))
    left_diag = lax.all_gather(left_tile, "col", axis=0, tiled=True)
    tri = jnp.sum(
        left_diag[:, :, None].astype(jnp.float32) * right_cols[:, None].astype(jnp.float32), axis=0
    )
    return finish(middle, tri, gate, w_out[1])


def solution(mesh):
    n = mesh.shape["row"]
    assert mesh.shape["col"] == n
    placed = (P("row", ("col", "ka"), None), P("row", ("col", "ka")), P(), P(), P())
    return jax.shard_map(
        lambda *a: on_device(n, *a),
        mesh=mesh,
        in_specs=placed,
        out_specs=P("row", ("col", "ka"), None),
        check_vma=False,
    )
```

```python
import jax
import jax.numpy as jnp
from jax import lax
from jax.sharding import PartitionSpec as P


def layer_norm(value):
    mean = jnp.mean(value, axis=-1, keepdims=True)
    centred = value - mean
    var = jnp.mean(centred * centred, axis=-1, keepdims=True)
    return centred / jnp.sqrt(var + 1e-05)


def prepare(pair, valid, weight_in, weight_gate):
    normed = layer_norm(pair.astype(jnp.float32)).astype(jnp.bfloat16)
    proj = jnp.einsum("ijc,cd->ijd", normed, weight_in, preferred_element_type=jnp.float32)
    width = proj.shape[-1] // 4
    left = (jax.nn.sigmoid(proj[..., :width]) * proj[..., width : 2 * width] * valid).astype(
        jnp.bfloat16
    )
    right = (
        jax.nn.sigmoid(proj[..., 2 * width : 3 * width]) * proj[..., 3 * width :] * valid
    ).astype(jnp.bfloat16)
    gate = jax.nn.sigmoid(
        jnp.einsum("ijc,cd->ijd", normed, weight_gate, preferred_element_type=jnp.float32)
    )
    return (left, right, gate)


def finish(pair, tri, gate, weight_out):
    normed = layer_norm(tri).astype(jnp.bfloat16)
    proj = jnp.einsum("ijc,cd->ijd", normed, weight_out, preferred_element_type=jnp.float32)
    return (pair.astype(jnp.float32) + gate * proj).astype(jnp.bfloat16)


def transpose_tiles(value, n):
    perm = [(r * n + c, c * n + r) for r in range(n) for c in range(n)]
    return lax.ppermute(value, ("row", "col"), perm)


def gather_a2a(value, axis_name, n, axis):
    copies = jnp.broadcast_to(value[None], (n,) + value.shape)
    got = lax.all_to_all(copies, axis_name, 0, 0, tiled=False)
    got = jnp.moveaxis(got, 0, axis)
    return got.reshape(value.shape[:axis] + (n * value.shape[axis],) + value.shape[axis + 1 :])


def sum_over_ka(partial_value):
    half = partial_value.shape[1] // 2
    me = lax.axis_index("ka")
    mine = lax.dynamic_slice_in_dim(partial_value, me * half, half, axis=1)
    theirs = lax.dynamic_slice_in_dim(partial_value, (1 - me) * half, half, axis=1)
    got = lax.ppermute(theirs.astype(jnp.bfloat16), "ka", [(0, 1), (1, 0)])
    return mine + got.astype(jnp.float32)


def join_over_ka(value):
    me = lax.axis_index("ka")
    got = lax.ppermute(value, "ka", [(0, 1), (1, 0)])
    return jnp.where(
        me == 0, jnp.concatenate([value, got], axis=1), jnp.concatenate([got, value], axis=1)
    )


def on_device(n, pair, pair_mask, w_in, w_gate, w_out):
    valid = pair_mask.astype(jnp.float32)[..., None]
    left, right, gate = prepare(pair, valid, w_in[0], w_gate[0])
    left_rows = lax.all_gather(jnp.swapaxes(left, 0, 1), "col", axis=0, tiled=True)
    right_diag = gather_a2a(jnp.swapaxes(transpose_tiles(right, n), 0, 1), "row", n, 0)
    partial_value = jnp.sum(
        left_rows[:, :, None].astype(jnp.float32) * right_diag[:, None].astype(jnp.float32),
        axis=0,
    )
    tri = sum_over_ka(partial_value)
    middle = finish(pair, tri, gate, w_out[0])
    left, right, gate = prepare(middle, valid, w_in[1], w_gate[1])
    right_cols = gather_a2a(right, "row", n, 0)
    left_tile = join_over_ka(transpose_tiles(left, n))
    left_diag = lax.all_gather(left_tile, "col", axis=0, tiled=True)
    tri = jnp.sum(
        left_diag[:, :, None].astype(jnp.float32) * right_cols[:, None].astype(jnp.float32), axis=0
    )
    return finish(middle, tri, gate, w_out[1])


def solution(mesh):
    n = mesh.shape["row"]
    assert mesh.shape["col"] == n
    placed = (P("row", ("col", "ka"), None), P("row", ("col", "ka")), P(), P(), P())
    return jax.shard_map(
        lambda *a: on_device(n, *a),
        mesh=mesh,
        in_specs=placed,
        out_specs=P("row", ("col", "ka"), None),
        check_vma=False,
    )
```

```python
import jax
import jax.numpy as jnp
from jax import lax
from jax.sharding import PartitionSpec as P


def layer_norm(value):
    mean = jnp.mean(value, axis=-1, keepdims=True)
    centred = value - mean
    var = jnp.mean(centred * centred, axis=-1, keepdims=True)
    return centred / jnp.sqrt(var + 1e-05)


def prepare(pair, valid, weight_in, weight_gate):
    normed = layer_norm(pair.astype(jnp.float32)).astype(jnp.bfloat16)
    proj = jnp.einsum("ijc,cd->ijd", normed, weight_in, preferred_element_type=jnp.float32)
    width = proj.shape[-1] // 4
    left = (jax.nn.sigmoid(proj[..., :width]) * proj[..., width : 2 * width] * valid).astype(
        jnp.bfloat16
    )
    right = (
        jax.nn.sigmoid(proj[..., 2 * width : 3 * width]) * proj[..., 3 * width :] * valid
    ).astype(jnp.bfloat16)
    gate = jax.nn.sigmoid(
        jnp.einsum("ijc,cd->ijd", normed, weight_gate, preferred_element_type=jnp.float32)
    )
    return (left, right, gate)


def finish(pair, tri, gate, weight_out):
    normed = layer_norm(tri).astype(jnp.bfloat16)
    proj = jnp.einsum("ijc,cd->ijd", normed, weight_out, preferred_element_type=jnp.float32)
    return (pair.astype(jnp.float32) + gate * proj).astype(jnp.bfloat16)


def transpose_tiles(value, n):
    perm = [(r * n + c, c * n + r) for r in range(n) for c in range(n)]
    return lax.ppermute(value, ("row", "col"), perm)


def gather_a2a(value, axis_name, n, axis):
    copies = jnp.broadcast_to(value[None], (n,) + value.shape)
    got = lax.all_to_all(copies, axis_name, 0, 0, tiled=False)
    got = jnp.moveaxis(got, 0, axis)
    return got.reshape(value.shape[:axis] + (n * value.shape[axis],) + value.shape[axis + 1 :])


def sum_over_ka(partial_value):
    half = partial_value.shape[1] // 2
    me = lax.axis_index("ka")
    mine = lax.dynamic_slice_in_dim(partial_value, me * half, half, axis=1)
    theirs = lax.dynamic_slice_in_dim(partial_value, (1 - me) * half, half, axis=1)
    got = lax.ppermute(theirs.astype(jnp.bfloat16), "ka", [(0, 1), (1, 0)])
    return mine + got.astype(jnp.float32)


def join_over_ka(value):
    me = lax.axis_index("ka")
    got = lax.ppermute(value, "ka", [(0, 1), (1, 0)])
    return jnp.where(
        me == 0, jnp.concatenate([value, got], axis=1), jnp.concatenate([got, value], axis=1)
    )


def gather_over_row(value, n):
    ny = n // 2
    me = lax.axis_index("row")
    swapped = lax.ppermute(value, "row", [(r, r ^ 1) for r in range(n)])
    pair = jnp.where(me % 2 == 0, jnp.stack([value, swapped]), jnp.stack([swapped, value]))
    fwd = [(r, ((r // 2 + 1) % ny) * 2 + r % 2) for r in range(n)]
    bwd = [(r, ((r // 2 - 1) % ny) * 2 + r % 2) for r in range(n)]
    plus, minus, got_plus, got_minus = pair, pair, [], []
    for step in range(1, ny // 2 + 1):
        plus = lax.ppermute(plus, "row", fwd)
        got_plus.append(plus)
        if step < ny - ny // 2:
            minus = lax.ppermute(minus, "row", bwd)
            got_minus.append(minus)
    stacked = jnp.stack([pair] + got_plus + got_minus[::-1])
    order = (me // 2 - jnp.arange(ny)) % ny
    blocks = jnp.take(stacked, order, axis=0)
    return blocks.reshape((n * value.shape[0],) + value.shape[1:])


def on_device(n, pair, pair_mask, w_in, w_gate, w_out):
    valid = pair_mask.astype(jnp.float32)[..., None]
    left, right, gate = prepare(pair, valid, w_in[0], w_gate[0])
    left_rows = lax.all_gather(jnp.swapaxes(left, 0, 1), "col", axis=0, tiled=True)
    right_diag = gather_over_row(jnp.swapaxes(transpose_tiles(right, n), 0, 1), n)
    partial_value = jnp.sum(
        left_rows[:, :, None].astype(jnp.float32) * right_diag[:, None].astype(jnp.float32),
        axis=0,
    )
    tri = sum_over_ka(partial_value)
    middle = finish(pair, tri, gate, w_out[0])
    left, right, gate = prepare(middle, valid, w_in[1], w_gate[1])
    right_cols = gather_over_row(right, n)
    left_tile = join_over_ka(transpose_tiles(left, n))
    left_diag = lax.all_gather(left_tile, "col", axis=0, tiled=True)
    tri = jnp.sum(
        left_diag[:, :, None].astype(jnp.float32) * right_cols[:, None].astype(jnp.float32), axis=0
    )
    return finish(middle, tri, gate, w_out[1])


def solution(mesh):
    n = mesh.shape["row"]
    assert mesh.shape["col"] == n
    placed = (P("row", ("col", "ka"), None), P("row", ("col", "ka")), P(), P(), P())
    return jax.shard_map(
        lambda *a: on_device(n, *a),
        mesh=mesh,
        in_specs=placed,
        out_specs=P("row", ("col", "ka"), None),
        check_vma=False,
    )
```

```python
import jax
import jax.numpy as jnp
from jax import lax
import numpy as np
from jax.sharding import Mesh, PartitionSpec as P

ROW, COL = ("y", "xl"), ("z", "core")


def layer_norm(value):
    mean = jnp.mean(value, axis=-1, keepdims=True)
    centred = value - mean
    var = jnp.mean(centred * centred, axis=-1, keepdims=True)
    return centred / jnp.sqrt(var + 1e-05)


def prepare(pair, valid, weight_in, weight_gate):
    normed = layer_norm(pair.astype(jnp.float32)).astype(jnp.bfloat16)
    proj = jnp.einsum("ijc,cd->ijd", normed, weight_in, preferred_element_type=jnp.float32)
    width = proj.shape[-1] // 4
    left = (jax.nn.sigmoid(proj[..., :width]) * proj[..., width : 2 * width] * valid).astype(
        jnp.bfloat16
    )
    right = (
        jax.nn.sigmoid(proj[..., 2 * width : 3 * width]) * proj[..., 3 * width :] * valid
    ).astype(jnp.bfloat16)
    gate = jax.nn.sigmoid(
        jnp.einsum("ijc,cd->ijd", normed, weight_gate, preferred_element_type=jnp.float32)
    )
    return (left, right, gate)


def finish(pair, tri, gate, weight_out):
    normed = layer_norm(tri).astype(jnp.bfloat16)
    proj = jnp.einsum("ijc,cd->ijd", normed, weight_out, preferred_element_type=jnp.float32)
    return (pair.astype(jnp.float32) + gate * proj).astype(jnp.bfloat16)


def transpose_tiles(value, n):
    perm = [(r * n + c, c * n + r) for r in range(n) for c in range(n)]
    return lax.ppermute(value, ROW + COL, perm)


def gather_a2a(value, axis_name, n, axis):
    copies = jnp.broadcast_to(value[None], (n,) + value.shape)
    got = lax.all_to_all(copies, axis_name, 0, 0, tiled=False)
    got = jnp.moveaxis(got, 0, axis)
    return got.reshape(value.shape[:axis] + (n * value.shape[axis],) + value.shape[axis + 1 :])


def sum_over_ka(partial_value):
    half = partial_value.shape[1] // 2
    me = lax.axis_index("ka")
    mine = lax.dynamic_slice_in_dim(partial_value, me * half, half, axis=1)
    theirs = lax.dynamic_slice_in_dim(partial_value, (1 - me) * half, half, axis=1)
    got = lax.ppermute(theirs.astype(jnp.bfloat16), "ka", [(0, 1), (1, 0)])
    return mine + got.astype(jnp.float32)


def join_over_ka(value):
    me = lax.axis_index("ka")
    got = lax.ppermute(value, "ka", [(0, 1), (1, 0)])
    return jnp.where(
        me == 0, jnp.concatenate([value, got], axis=1), jnp.concatenate([got, value], axis=1)
    )


def gather_over_row(value):
    me = lax.axis_index("xl")
    swapped = lax.ppermute(value, "xl", [(0, 1), (1, 0)])
    pair = jnp.where(me == 0, jnp.stack([value, swapped]), jnp.stack([swapped, value]))
    ny = lax.psum(1, "y")
    copies = jnp.broadcast_to(pair[None], (ny,) + pair.shape)
    got = lax.all_to_all(copies, "y", 0, 0, tiled=False)
    return got.reshape((2 * ny * value.shape[0],) + value.shape[1:])


def on_device(n, pair, pair_mask, w_in, w_gate, w_out):
    valid = pair_mask.astype(jnp.float32)[..., None]
    left, right, gate = prepare(pair, valid, w_in[0], w_gate[0])
    left_rows = lax.all_gather(jnp.swapaxes(left, 0, 1), COL, axis=0, tiled=True)
    right_diag = gather_over_row(jnp.swapaxes(transpose_tiles(right, n), 0, 1))
    partial_value = jnp.sum(
        left_rows[:, :, None].astype(jnp.float32) * right_diag[:, None].astype(jnp.float32),
        axis=0,
    )
    tri = sum_over_ka(partial_value)
    middle = finish(pair, tri, gate, w_out[0])
    left, right, gate = prepare(middle, valid, w_in[1], w_gate[1])
    right_cols = gather_over_row(right)
    left_tile = join_over_ka(transpose_tiles(left, n))
    left_diag = lax.all_gather(left_tile, COL, axis=0, tiled=True)
    tri = jnp.sum(
        left_diag[:, :, None].astype(jnp.float32) * right_cols[:, None].astype(jnp.float32), axis=0
    )
    return finish(middle, tri, gate, w_out[1])


def solution(mesh):
    n = mesh.shape["row"]
    assert mesh.shape["col"] == n
    devices = np.asarray(mesh.devices).reshape(n // 2, 2, n // 2, 2, mesh.shape["ka"])
    fine = Mesh(devices, ("y", "xl", "z", "core", "ka"))
    placed = (P(ROW, COL + ("ka",), None), P(ROW, COL + ("ka",)), P(), P(), P())
    return jax.shard_map(
        lambda *a: on_device(n, *a),
        mesh=fine,
        in_specs=placed,
        out_specs=P(ROW, COL + ("ka",), None),
        check_vma=False,
    )
```

```python
import jax
import jax.numpy as jnp
from jax import lax
from jax.sharding import PartitionSpec as P


def layer_norm(value):
    mean = jnp.mean(value, axis=-1, keepdims=True)
    centred = value - mean
    var = jnp.mean(centred * centred, axis=-1, keepdims=True)
    return centred / jnp.sqrt(var + 1e-05)


def prepare(pair, valid, weight_in, weight_gate):
    normed = layer_norm(pair.astype(jnp.float32)).astype(jnp.bfloat16)
    proj = jnp.einsum("ijc,cd->ijd", normed, weight_in, preferred_element_type=jnp.float32)
    width = proj.shape[-1] // 4
    left = (jax.nn.sigmoid(proj[..., :width]) * proj[..., width : 2 * width] * valid).astype(
        jnp.bfloat16
    )
    right = (
        jax.nn.sigmoid(proj[..., 2 * width : 3 * width]) * proj[..., 3 * width :] * valid
    ).astype(jnp.bfloat16)
    gate = jax.nn.sigmoid(
        jnp.einsum("ijc,cd->ijd", normed, weight_gate, preferred_element_type=jnp.float32)
    )
    return (left, right, gate)


def finish(pair, tri, gate, weight_out):
    normed = layer_norm(tri).astype(jnp.bfloat16)
    proj = jnp.einsum("ijc,cd->ijd", normed, weight_out, preferred_element_type=jnp.float32)
    return (pair.astype(jnp.float32) + gate * proj).astype(jnp.bfloat16)


def transpose_tiles(value, n):
    perm = [(r * n + c, c * n + r) for r in range(n) for c in range(n)]
    return lax.ppermute(value, ("row", "col"), perm)


def gather_a2a(value, axis_name, n, axis):
    copies = jnp.broadcast_to(value[None], (n,) + value.shape)
    got = lax.all_to_all(copies, axis_name, 0, 0, tiled=False)
    got = jnp.moveaxis(got, 0, axis)
    return got.reshape(value.shape[:axis] + (n * value.shape[axis],) + value.shape[axis + 1 :])


def sum_over_ka(partial_value):
    half = partial_value.shape[1] // 2
    me = lax.axis_index("ka")
    mine = lax.dynamic_slice_in_dim(partial_value, me * half, half, axis=1)
    theirs = lax.dynamic_slice_in_dim(partial_value, (1 - me) * half, half, axis=1)
    got = lax.ppermute(theirs.astype(jnp.bfloat16), "ka", [(0, 1), (1, 0)])
    return mine + got.astype(jnp.float32)


def join_over_ka(value):
    me = lax.axis_index("ka")
    got = lax.ppermute(value, "ka", [(0, 1), (1, 0)])
    return jnp.where(
        me == 0, jnp.concatenate([value, got], axis=1), jnp.concatenate([got, value], axis=1)
    )


def on_device(n, pair, pair_mask, w_in, w_gate, w_out):
    valid = pair_mask.astype(jnp.float32)[..., None]
    left, right, gate = prepare(pair, valid, w_in[0], w_gate[0])
    left_rows = lax.all_gather(jnp.swapaxes(left, 0, 1), "col", axis=0, tiled=True)
    right_diag = gather_a2a(jnp.swapaxes(transpose_tiles(right, n), 0, 1), "row", n, 0)
    half = right_diag.shape[1] // 2
    me = lax.axis_index("ka")
    theirs = lax.dynamic_slice_in_dim(right_diag, (1 - me) * half, half, axis=1)
    mine = lax.dynamic_slice_in_dim(right_diag, me * half, half, axis=1)
    sent = jnp.sum(
        left_rows[:, :, None].astype(jnp.float32) * theirs[:, None].astype(jnp.float32), axis=0
    ).astype(jnp.bfloat16)
    sent, left_later, mine = lax.optimization_barrier((sent, left_rows, mine))
    got = lax.ppermute(sent, "ka", [(0, 1), (1, 0)])
    kept = jnp.sum(
        left_later[:, :, None].astype(jnp.float32) * mine[:, None].astype(jnp.float32), axis=0
    )
    tri = kept + got.astype(jnp.float32)
    middle = finish(pair, tri, gate, w_out[0])
    left, right, gate = prepare(middle, valid, w_in[1], w_gate[1])
    right_cols = gather_a2a(right, "row", n, 0)
    left_tile = join_over_ka(transpose_tiles(left, n))
    left_diag = lax.all_gather(left_tile, "col", axis=0, tiled=True)
    tri = jnp.sum(
        left_diag[:, :, None].astype(jnp.float32) * right_cols[:, None].astype(jnp.float32), axis=0
    )
    return finish(middle, tri, gate, w_out[1])


def solution(mesh):
    n = mesh.shape["row"]
    assert mesh.shape["col"] == n
    placed = (P("row", ("col", "ka"), None), P("row", ("col", "ka")), P(), P(), P())
    return jax.shard_map(
        lambda *a: on_device(n, *a),
        mesh=mesh,
        in_specs=placed,
        out_specs=P("row", ("col", "ka"), None),
        check_vma=False,
    )
```

```python
import jax
import jax.numpy as jnp
from jax import lax
from jax.sharding import PartitionSpec as P


def layer_norm(value):
    mean = jnp.mean(value, axis=-1, keepdims=True)
    centred = value - mean
    var = jnp.mean(centred * centred, axis=-1, keepdims=True)
    return centred / jnp.sqrt(var + 1e-05)


def prepare(pair, valid, weight_in, weight_gate):
    normed = layer_norm(pair.astype(jnp.float32)).astype(jnp.bfloat16)
    proj = jnp.einsum("ijc,cd->ijd", normed, weight_in, preferred_element_type=jnp.float32)
    width = proj.shape[-1] // 4
    left = (jax.nn.sigmoid(proj[..., :width]) * proj[..., width : 2 * width] * valid).astype(
        jnp.bfloat16
    )
    right = (
        jax.nn.sigmoid(proj[..., 2 * width : 3 * width]) * proj[..., 3 * width :] * valid
    ).astype(jnp.bfloat16)
    gate = jax.nn.sigmoid(
        jnp.einsum("ijc,cd->ijd", normed, weight_gate, preferred_element_type=jnp.float32)
    )
    return (left, right, gate)


def finish(pair, tri, gate, weight_out):
    normed = layer_norm(tri).astype(jnp.bfloat16)
    proj = jnp.einsum("ijc,cd->ijd", normed, weight_out, preferred_element_type=jnp.float32)
    return (pair.astype(jnp.float32) + gate * proj).astype(jnp.bfloat16)


def transpose_tiles(value, n):
    perm = [(r * n + c, c * n + r) for r in range(n) for c in range(n)]
    return lax.ppermute(value, ("row", "col"), perm)


def gather_a2a(value, axis_name, n, axis):
    copies = jnp.broadcast_to(value[None], (n,) + value.shape)
    got = lax.all_to_all(copies, axis_name, 0, 0, tiled=False)
    got = jnp.moveaxis(got, 0, axis)
    return got.reshape(value.shape[:axis] + (n * value.shape[axis],) + value.shape[axis + 1 :])


def sum_over_ka(partial_value):
    half = partial_value.shape[1] // 2
    me = lax.axis_index("ka")
    mine = lax.dynamic_slice_in_dim(partial_value, me * half, half, axis=1)
    theirs = lax.dynamic_slice_in_dim(partial_value, (1 - me) * half, half, axis=1)
    got = lax.ppermute(theirs.astype(jnp.bfloat16), "ka", [(0, 1), (1, 0)])
    return mine + got.astype(jnp.float32)


def join_over_ka(value):
    me = lax.axis_index("ka")
    got = lax.ppermute(value, "ka", [(0, 1), (1, 0)])
    return jnp.where(
        me == 0, jnp.concatenate([value, got], axis=1), jnp.concatenate([got, value], axis=1)
    )


def on_device(n, pair, pair_mask, w_in, w_gate, w_out):
    valid = pair_mask.astype(jnp.float32)[..., None]
    left, right, gate = prepare(pair, valid, w_in[0], w_gate[0])
    left_rows = lax.all_gather(jnp.swapaxes(left, 0, 1), "col", axis=0, tiled=True)
    right_diag = gather_a2a(jnp.swapaxes(transpose_tiles(right, n), 0, 1), "row", n, 0)
    half = right_diag.shape[1] // 2
    me = lax.axis_index("ka")
    theirs = lax.dynamic_slice_in_dim(right_diag, (1 - me) * half, half, axis=1)
    mine = lax.dynamic_slice_in_dim(right_diag, me * half, half, axis=1)
    sent = jnp.sum(left_rows[:, :, None] * theirs[:, None], axis=0, dtype=jnp.float32).astype(
        jnp.bfloat16
    )
    sent, left_later, mine = lax.optimization_barrier((sent, left_rows, mine))
    got = lax.ppermute(sent, "ka", [(0, 1), (1, 0)])
    kept = jnp.sum(left_later[:, :, None] * mine[:, None], axis=0, dtype=jnp.float32)
    tri = kept + got.astype(jnp.float32)
    middle = finish(pair, tri, gate, w_out[0])
    left, right, gate = prepare(middle, valid, w_in[1], w_gate[1])
    right_cols = gather_a2a(right, "row", n, 0)
    left_tile = join_over_ka(transpose_tiles(left, n))
    left_diag = lax.all_gather(left_tile, "col", axis=0, tiled=True)
    tri = jnp.sum(left_diag[:, :, None] * right_cols[:, None], axis=0, dtype=jnp.float32)
    return finish(middle, tri, gate, w_out[1])


def solution(mesh):
    n = mesh.shape["row"]
    assert mesh.shape["col"] == n
    placed = (P("row", ("col", "ka"), None), P("row", ("col", "ka")), P(), P(), P())
    return jax.shard_map(
        lambda *a: on_device(n, *a),
        mesh=mesh,
        in_specs=placed,
        out_specs=P("row", ("col", "ka"), None),
        check_vma=False,
    )
```

```python
import jax
import jax.numpy as jnp
from jax import lax
from jax.sharding import PartitionSpec as P


def layer_norm(value):
    mean = jnp.mean(value, axis=-1, keepdims=True)
    centred = value - mean
    var = jnp.mean(centred * centred, axis=-1, keepdims=True)
    return centred / jnp.sqrt(var + 1e-05)


def prepare(pair, valid, weight_in, weight_gate):
    normed = layer_norm(pair.astype(jnp.float32)).astype(jnp.bfloat16)
    proj = jnp.einsum("ijc,cd->ijd", normed, weight_in, preferred_element_type=jnp.float32)
    width = proj.shape[-1] // 4
    left = (jax.nn.sigmoid(proj[..., :width]) * proj[..., width : 2 * width] * valid).astype(
        jnp.bfloat16
    )
    right = (
        jax.nn.sigmoid(proj[..., 2 * width : 3 * width]) * proj[..., 3 * width :] * valid
    ).astype(jnp.bfloat16)
    gate = jax.nn.sigmoid(
        jnp.einsum("ijc,cd->ijd", normed, weight_gate, preferred_element_type=jnp.float32)
    )
    return (left, right, gate)


def finish(pair, tri, gate, weight_out):
    normed = layer_norm(tri).astype(jnp.bfloat16)
    proj = jnp.einsum("ijc,cd->ijd", normed, weight_out, preferred_element_type=jnp.float32)
    return (pair.astype(jnp.float32) + gate * proj).astype(jnp.bfloat16)


def transpose_tiles(value, n):
    perm = [(r * n + c, c * n + r) for r in range(n) for c in range(n)]
    return lax.ppermute(value, ("row", "col"), perm)


def gather_a2a(value, axis_name, n, axis):
    copies = jnp.broadcast_to(value[None], (n,) + value.shape)
    got = lax.all_to_all(copies, axis_name, 0, 0, tiled=False)
    got = jnp.moveaxis(got, 0, axis)
    return got.reshape(value.shape[:axis] + (n * value.shape[axis],) + value.shape[axis + 1 :])


def sum_over_ka(partial_value):
    half = partial_value.shape[1] // 2
    me = lax.axis_index("ka")
    mine = lax.dynamic_slice_in_dim(partial_value, me * half, half, axis=1)
    theirs = lax.dynamic_slice_in_dim(partial_value, (1 - me) * half, half, axis=1)
    got = lax.ppermute(theirs.astype(jnp.bfloat16), "ka", [(0, 1), (1, 0)])
    return mine + got.astype(jnp.float32)


def join_over_ka(value):
    me = lax.axis_index("ka")
    got = lax.ppermute(value, "ka", [(0, 1), (1, 0)])
    return jnp.where(
        me == 0, jnp.concatenate([value, got], axis=1), jnp.concatenate([got, value], axis=1)
    )


def on_device(n, pair, pair_mask, w_in, w_gate, w_out):
    valid = pair_mask.astype(jnp.float32)[..., None]
    left, right, gate = prepare(pair, valid, w_in[0], w_gate[0])
    few = 2
    left_t = jnp.swapaxes(left, 0, 1)
    right_t = jnp.swapaxes(transpose_tiles(right, n), 0, 1)
    width = left_t.shape[0]
    left_all = lax.all_gather(left_t, "col", axis=0, tiled=False)
    right_few = lax.all_gather(right_t[:few], "row", axis=0, tiled=True)
    right_rest = gather_a2a(right_t[few:], "row", n, 0)
    left_few = left_all[:, :few].reshape((n * few,) + left_t.shape[1:])
    left_rest = left_all[:, few:].reshape((n * (width - few),) + left_t.shape[1:])
    half = right_t.shape[1] // 2
    me = lax.axis_index("ka")

    def part_sum(lhs, rhs, start):
        cut = lax.dynamic_slice_in_dim(rhs, start, half, axis=1)
        return jnp.sum(
            lhs[:, :, None].astype(jnp.float32) * cut[:, None].astype(jnp.float32), axis=0
        )

    sent = (
        part_sum(left_few, right_few, (1 - me) * half)
        + part_sum(left_rest, right_rest, (1 - me) * half)
    ).astype(jnp.bfloat16)
    sent, left_few, left_rest, right_few, right_rest = lax.optimization_barrier(
        (sent, left_few, left_rest, right_few, right_rest)
    )
    got = lax.ppermute(sent, "ka", [(0, 1), (1, 0)])
    kept = part_sum(left_few, right_few, me * half) + part_sum(left_rest, right_rest, me * half)
    tri = kept + got.astype(jnp.float32)
    middle = finish(pair, tri, gate, w_out[0])
    left, right, gate = prepare(middle, valid, w_in[1], w_gate[1])
    right_cols = gather_a2a(right, "row", n, 0)
    left_tile = join_over_ka(transpose_tiles(left, n))
    left_diag = lax.all_gather(left_tile, "col", axis=0, tiled=True)
    tri = jnp.sum(
        left_diag[:, :, None].astype(jnp.float32) * right_cols[:, None].astype(jnp.float32), axis=0
    )
    return finish(middle, tri, gate, w_out[1])


def solution(mesh):
    n = mesh.shape["row"]
    assert mesh.shape["col"] == n
    placed = (P("row", ("col", "ka"), None), P("row", ("col", "ka")), P(), P(), P())
    return jax.shard_map(
        lambda *a: on_device(n, *a),
        mesh=mesh,
        in_specs=placed,
        out_specs=P("row", ("col", "ka"), None),
        check_vma=False,
    )
```

```python
import jax
import jax.numpy as jnp
from jax import lax
from jax.sharding import PartitionSpec as P


def layer_norm(value):
    mean = jnp.mean(value, axis=-1, keepdims=True)
    centred = value - mean
    var = jnp.mean(centred * centred, axis=-1, keepdims=True)
    return centred / jnp.sqrt(var + 1e-05)


def prepare(pair, valid, weight_in, weight_gate):
    normed = layer_norm(pair.astype(jnp.float32)).astype(jnp.bfloat16)
    proj = jnp.einsum("ijc,cd->ijd", normed, weight_in, preferred_element_type=jnp.float32)
    width = proj.shape[-1] // 4
    left = (jax.nn.sigmoid(proj[..., :width]) * proj[..., width : 2 * width] * valid).astype(
        jnp.bfloat16
    )
    right = (
        jax.nn.sigmoid(proj[..., 2 * width : 3 * width]) * proj[..., 3 * width :] * valid
    ).astype(jnp.bfloat16)
    gate = jax.nn.sigmoid(
        jnp.einsum("ijc,cd->ijd", normed, weight_gate, preferred_element_type=jnp.float32)
    )
    return (left, right, gate)


def finish(pair, tri, gate, weight_out):
    normed = layer_norm(tri).astype(jnp.bfloat16)
    proj = jnp.einsum("ijc,cd->ijd", normed, weight_out, preferred_element_type=jnp.float32)
    return (pair.astype(jnp.float32) + gate * proj).astype(jnp.bfloat16)


def transpose_tiles(value, n):
    perm = [(r * n + c, c * n + r) for r in range(n) for c in range(n)]
    return lax.ppermute(value, ("row", "col"), perm)


def gather_a2a(value, axis_name, n, axis):
    copies = jnp.broadcast_to(value[None], (n,) + value.shape)
    got = lax.all_to_all(copies, axis_name, 0, 0, tiled=False)
    got = jnp.moveaxis(got, 0, axis)
    return got.reshape(value.shape[:axis] + (n * value.shape[axis],) + value.shape[axis + 1 :])


def sum_over_ka(partial_value):
    half = partial_value.shape[1] // 2
    me = lax.axis_index("ka")
    mine = lax.dynamic_slice_in_dim(partial_value, me * half, half, axis=1)
    theirs = lax.dynamic_slice_in_dim(partial_value, (1 - me) * half, half, axis=1)
    got = lax.ppermute(theirs.astype(jnp.bfloat16), "ka", [(0, 1), (1, 0)])
    return mine + got.astype(jnp.float32)


def join_over_ka(value):
    me = lax.axis_index("ka")
    got = lax.ppermute(value, "ka", [(0, 1), (1, 0)])
    return jnp.where(
        me == 0, jnp.concatenate([value, got], axis=1), jnp.concatenate([got, value], axis=1)
    )


def on_device(n, pair, pair_mask, w_in, w_gate, w_out):
    valid = pair_mask.astype(jnp.float32)[..., None]
    left, right, gate = prepare(pair, valid, w_in[0], w_gate[0])
    left_rows = lax.all_gather(jnp.swapaxes(left, 0, 1), "col", axis=0, tiled=True)
    right_diag = gather_a2a(jnp.swapaxes(transpose_tiles(right, n), 0, 1), "row", n, 0)
    half = right_diag.shape[1] // 2
    me = lax.axis_index("ka")
    theirs = lax.dynamic_slice_in_dim(right_diag, (1 - me) * half, half, axis=1)
    mine = lax.dynamic_slice_in_dim(right_diag, me * half, half, axis=1)
    sent = jnp.sum(
        left_rows[:, :, None].astype(jnp.float32) * theirs[:, None].astype(jnp.float32), axis=0
    ).astype(jnp.bfloat16)
    sent, left_later, mine = lax.optimization_barrier((sent, left_rows, mine))
    got = lax.ppermute(sent, "ka", [(0, 1), (1, 0)])
    kept = jnp.sum(
        left_later[:, :, None].astype(jnp.float32) * mine[:, None].astype(jnp.float32), axis=0
    )
    tri = kept + got.astype(jnp.float32)
    middle = finish(pair, tri, gate, w_out[0])
    left, right, gate = prepare(middle, valid, w_in[1], w_gate[1])
    right_cols = gather_a2a(right, "row", n, 0)
    left_tile = join_over_ka(transpose_tiles(left, n))
    left_diag = lax.all_gather(left_tile, "col", axis=0, tiled=True)
    tri = jnp.sum(left_diag[:, :, None] * right_cols[:, None], axis=0, dtype=jnp.float32)
    return finish(middle, tri, gate, w_out[1])


def solution(mesh):
    n = mesh.shape["row"]
    assert mesh.shape["col"] == n
    placed = (P("row", ("col", "ka"), None), P("row", ("col", "ka")), P(), P(), P())
    return jax.shard_map(
        lambda *a: on_device(n, *a),
        mesh=mesh,
        in_specs=placed,
        out_specs=P("row", ("col", "ka"), None),
        check_vma=False,
    )
```

```python
import jax
import jax.numpy as jnp
from jax import lax
from jax.sharding import PartitionSpec as P


def layer_norm(value):
    mean = jnp.mean(value, axis=-1, keepdims=True)
    centred = value - mean
    var = jnp.mean(centred * centred, axis=-1, keepdims=True)
    return centred / jnp.sqrt(var + 1e-05)


def prepare(pair, valid, weight_in, weight_gate):
    normed = layer_norm(pair.astype(jnp.float32)).astype(jnp.bfloat16)
    proj = jnp.einsum("ijc,cd->ijd", normed, weight_in, preferred_element_type=jnp.float32)
    width = proj.shape[-1] // 4
    left = (jax.nn.sigmoid(proj[..., :width]) * proj[..., width : 2 * width] * valid).astype(
        jnp.bfloat16
    )
    right = (
        jax.nn.sigmoid(proj[..., 2 * width : 3 * width]) * proj[..., 3 * width :] * valid
    ).astype(jnp.bfloat16)
    gate = jax.nn.sigmoid(
        jnp.einsum("ijc,cd->ijd", normed, weight_gate, preferred_element_type=jnp.float32)
    )
    return (left, right, gate)


def finish(pair, tri, gate, weight_out):
    normed = layer_norm(tri).astype(jnp.bfloat16)
    proj = jnp.einsum("ijc,cd->ijd", normed, weight_out, preferred_element_type=jnp.float32)
    return (pair.astype(jnp.float32) + gate * proj).astype(jnp.bfloat16)


def transpose_tiles(value, n):
    perm = [(r * n + c, c * n + r) for r in range(n) for c in range(n)]
    return lax.ppermute(value, ("row", "col"), perm)


def gather_a2a(value, axis_name, n, axis):
    copies = jnp.broadcast_to(value[None], (n,) + value.shape)
    got = lax.all_to_all(copies, axis_name, 0, 0, tiled=False)
    got = jnp.moveaxis(got, 0, axis)
    return got.reshape(value.shape[:axis] + (n * value.shape[axis],) + value.shape[axis + 1 :])


def sum_over_ka(partial_value):
    half = partial_value.shape[1] // 2
    me = lax.axis_index("ka")
    mine = lax.dynamic_slice_in_dim(partial_value, me * half, half, axis=1)
    theirs = lax.dynamic_slice_in_dim(partial_value, (1 - me) * half, half, axis=1)
    got = lax.ppermute(theirs.astype(jnp.bfloat16), "ka", [(0, 1), (1, 0)])
    return mine + got.astype(jnp.float32)


def join_over_ka(value):
    me = lax.axis_index("ka")
    got = lax.ppermute(value, "ka", [(0, 1), (1, 0)])
    return jnp.where(
        me == 0, jnp.concatenate([value, got], axis=1), jnp.concatenate([got, value], axis=1)
    )


def transposed_tile(value, n):
    me = lax.axis_index("ka")
    own = transpose_tiles(value, n)
    perm = [
        ((c * n + r) * 2 + 1 - k, (r * n + c) * 2 + k)
        for r in range(n)
        for c in range(n)
        for k in range(2)
    ]
    other = lax.ppermute(value, ("row", "col", "ka"), perm)
    return jnp.where(
        me == 0, jnp.concatenate([own, other], axis=1), jnp.concatenate([other, own], axis=1)
    )


def on_device(n, pair, pair_mask, w_in, w_gate, w_out):
    valid = pair_mask.astype(jnp.float32)[..., None]
    left, right, gate = prepare(pair, valid, w_in[0], w_gate[0])
    left_rows = lax.all_gather(jnp.swapaxes(left, 0, 1), "col", axis=0, tiled=True)
    right_diag = gather_a2a(jnp.swapaxes(transpose_tiles(right, n), 0, 1), "row", n, 0)
    half = right_diag.shape[1] // 2
    me = lax.axis_index("ka")
    theirs = lax.dynamic_slice_in_dim(right_diag, (1 - me) * half, half, axis=1)
    mine = lax.dynamic_slice_in_dim(right_diag, me * half, half, axis=1)
    sent = jnp.sum(
        left_rows[:, :, None].astype(jnp.float32) * theirs[:, None].astype(jnp.float32), axis=0
    ).astype(jnp.bfloat16)
    sent, left_later, mine = lax.optimization_barrier((sent, left_rows, mine))
    got = lax.ppermute(sent, "ka", [(0, 1), (1, 0)])
    kept = jnp.sum(
        left_later[:, :, None].astype(jnp.float32) * mine[:, None].astype(jnp.float32), axis=0
    )
    tri = kept + got.astype(jnp.float32)
    middle = finish(pair, tri, gate, w_out[0])
    left, right, gate = prepare(middle, valid, w_in[1], w_gate[1])
    right_cols = gather_a2a(right, "row", n, 0)
    left_tile = transposed_tile(left, n)
    left_diag = lax.all_gather(left_tile, "col", axis=0, tiled=True)
    tri = jnp.sum(left_diag[:, :, None] * right_cols[:, None], axis=0, dtype=jnp.float32)
    return finish(middle, tri, gate, w_out[1])


def solution(mesh):
    n = mesh.shape["row"]
    assert mesh.shape["col"] == n
    placed = (P("row", ("col", "ka"), None), P("row", ("col", "ka")), P(), P(), P())
    return jax.shard_map(
        lambda *a: on_device(n, *a),
        mesh=mesh,
        in_specs=placed,
        out_specs=P("row", ("col", "ka"), None),
        check_vma=False,
    )
```
